256 devices in a mesh: vgrp: 4 (over y), samp: 64 (over z, x, core).
Axes of the slice: x: 4, y: 4, z: 8, core: 2. Of those that a mesh axis runs over, the one named last changes fastest.
Arguments:
- phenotype: float32 [196608], P(('vgrp', 'samp')), may hold values from -6 to 6
- exposures: float32 [196608, 128], P('samp'), may hold values from -6 to 6
- perms: int32 [16, 196608], P(None, 'samp'), may hold values from 0 to 196607, each once within a row
- genotypes: int32 [196608, 2048], P('samp', 'vgrp'), may hold values from 0 to 2
Outputs:
- statistics: float32 [2048, 16], P(('vgrp', 'samp'))
The draws below stay inside these ranges and needn't reach their ends.
Inputs may be any that keep to these rules, and one draw needn't show every extreme that they name: Each row of perms holds every sample index once.
All inputs are finite; a program needn't handle non-finite values.
Results may differ from the reference program's by a relative error of at most 0.00075.
Values sent between devices are 32-bit elements; how exact they have to be, the bound alone decides.
No kernel may reach another device: no remote copies, remote signals or barrier semaphores. Data moves between devices by JAX's collectives and lax.ppermute only.
A program may use at most 64 MiB of HBM per device.

```python
import jax
import jax.numpy as jnp
from jax import lax

EXPO = 128
PERMS = 16
VARIANTS = 2048
SAMPLES = 196608


def touch_ends(entries, key, smallest, top_value):
    longest = entries.shape.index(max(entries.shape))
    spots = []
    for shift in (0, 1):
        where = [jax.random.randint(jax.random.fold_in(key, axis), (), 0, length) for axis, length in enumerate(entries.shape)]
        where[longest] = (where[longest] + shift) % entries.shape[longest]
        spots.append(tuple(where))
    return entries.at[spots[0]].set(smallest).at[spots[1]].set(top_value)


def level_of(stream_key, extent, pieces, smallest, largest):
    def one(dim, shards_of):
        draws = jax.random.uniform(jax.random.fold_in(jax.random.fold_in(stream_key, 6), dim), (shards_of,), jnp.float32, smallest / len(pieces), largest / len(pieces))
        return jnp.repeat(jnp.exp(draws), extent[dim] // shards_of).reshape((-1,) + (1,) * (len(extent) - dim - 1))

    factor_of = one(*pieces[0])
    for cut in pieces[1:]:
        factor_of = factor_of * one(*cut)
    return factor_of


def normal_values(own_key, shape, width, reach, pieces=(), held_as=jnp.bfloat16):
    result = width * jax.random.normal(own_key, shape, jnp.float32)
    if pieces:
        result = result * level_of(own_key, shape, pieces, -0.22, 0.18)
    return jnp.clip(result, -reach, reach).astype(held_as)


def setup_inputs(seed: int = 0) -> dict:
    key_list = jax.random.split(jax.random.key(seed), 5)
    return {
        "phenotype": normal_values(key_list[0], (SAMPLES,), 1.0, 6.0, ((0, 256),), jnp.float32),
        "exposures": normal_values(key_list[1], (SAMPLES, EXPO), 1.0, 6.0, ((0, 64),), jnp.float32),
        "perms": jax.vmap(lambda own: jax.random.permutation(own, SAMPLES))(jax.random.split(key_list[2], PERMS)).reshape((PERMS, SAMPLES)).astype(jnp.int32),
        "genotypes": touch_ends(jax.random.randint(key_list[3], (SAMPLES, VARIANTS), 0, 3), jax.random.fold_in(key_list[3], 1), 0, 2).astype(jnp.int32),
    }


def chol_solve(factor, rhs):
    middle = lax.linalg.triangular_solve(factor, rhs, left_side=True, lower=True)
    return lax.linalg.triangular_solve(factor, middle, left_side=True, lower=True, transpose_a=True)

def reference(phenotype, exposures, perms, genotypes):
    hi = lax.Precision.HIGHEST
    permuted = jnp.transpose(phenotype[perms])
    gram = jnp.dot(exposures.T, exposures, precision=hi)
    cross = jnp.dot(exposures.T, permuted, precision=hi)
    system = gram + 0.5 * SAMPLES * jnp.eye(EXPO, dtype=jnp.float32)
    factor = jnp.linalg.cholesky(system)
    coefficients = chol_solve(factor, cross)
    residuals = permuted - jnp.dot(exposures, coefficients, precision=hi)
    weighted = (exposures[:, :, None] * residuals[:, None, :]).reshape(SAMPLES, EXPO * PERMS).astype(jnp.bfloat16)
    dosages = genotypes.astype(jnp.bfloat16)
    scores = jnp.dot(dosages.T.astype(jnp.float32), weighted.astype(jnp.float32), preferred_element_type=jnp.float32)
    scores = scores.reshape(VARIANTS, EXPO, PERMS)
    return jnp.sum(scores * scores, axis=1) / (SAMPLES * EXPO)
```

```python
import jax
import jax.numpy as jnp
from jax import lax
from jax.sharding import PartitionSpec as P


def chol_solve(factor, rhs):
    middle = lax.linalg.triangular_solve(factor, rhs, left_side=True, lower=True)
    return lax.linalg.triangular_solve(factor, middle, left_side=True, lower=True, transpose_a=True)


def per_device(phenotype, exposures, perms, genotypes):
    hi = lax.Precision.HIGHEST
    nv = lax.axis_size("vgrp")
    local_rows = exposures.shape[0]
    width = exposures.shape[1]
    quarter = local_rows // nv
    offset_rows = lax.axis_index("vgrp") * quarter
    expo_part = lax.dynamic_slice_in_dim(exposures, offset_rows, quarter, 0)
    gram_part = jnp.dot(expo_part.T, expo_part, precision=hi)
    gram = lax.psum(gram_part, ("vgrp", "samp"))
    pheno_full = lax.all_gather(phenotype, ("vgrp", "samp"), axis=0, tiled=True)
    samples = pheno_full.shape[0]
    system = gram + 0.5 * samples * jnp.eye(width, dtype=jnp.float32)
    factor = jnp.linalg.cholesky(system)
    perm_part = lax.dynamic_slice_in_dim(perms, offset_rows, quarter, 1)
    pheno_part = jnp.take(pheno_full, perm_part.T, axis=0, mode="clip")
    cross_part = jnp.dot(expo_part.T, pheno_part, precision=hi)
    cross = lax.psum(cross_part, ("vgrp", "samp"))
    coefficients = chol_solve(factor, cross)
    permuted = lax.all_gather(pheno_part, "vgrp", axis=0, tiled=True)
    residuals = permuted - jnp.dot(exposures, coefficients, precision=hi)
    nperm = residuals.shape[1]
    weighted = (
        (exposures[:, :, None] * residuals[:, None, :])
        .reshape(local_rows, width * nperm)
        .astype(jnp.bfloat16)
    )
    dosages = genotypes.astype(jnp.bfloat16)
    partial = jnp.dot(dosages.T, weighted, preferred_element_type=jnp.float32)
    own_scores = lax.psum_scatter(partial, "samp", scatter_dimension=0, tiled=True)
    own_rows = own_scores.shape[0]
    shaped = own_scores.reshape(own_rows, width, nperm)
    return jnp.sum(shaped * shaped, axis=1) / (samples * width)


def solution(mesh):
    return jax.shard_map(
        per_device,
        mesh=mesh,
        in_specs=(P(("vgrp", "samp")), P("samp", None), P(None, "samp"), P("samp", "vgrp")),
        out_specs=P(("vgrp", "samp"), None),
        check_vma=False,
    )
```

```python
import jax
import jax.numpy as jnp
from jax import lax
from jax.sharding import Mesh, PartitionSpec as P

SAMP = ("z", "x", "core")
ALL = ("vgrp",) + SAMP


def chol_solve(factor, rhs):
    middle = lax.linalg.triangular_solve(factor, rhs, left_side=True, lower=True)
    return lax.linalg.triangular_solve(factor, middle, left_side=True, lower=True, transpose_a=True)


def staged_psum(x):
    for axis in ("core", "x", "z", "vgrp"):
        x = lax.psum(x, axis)
    return x


def per_device(phenotype, exposures, perms, genotypes):
    hi = lax.Precision.HIGHEST
    nv = lax.axis_size("vgrp")
    local_rows = exposures.shape[0]
    width = exposures.shape[1]
    quarter = local_rows // nv
    offset_rows = lax.axis_index("vgrp") * quarter
    expo_part = lax.dynamic_slice_in_dim(exposures, offset_rows, quarter, 0)
    gram_part = jnp.dot(expo_part.T, expo_part, precision=hi)
    gram = staged_psum(gram_part)
    pheno_full = phenotype
    for axis in ("core", "x", "z", "vgrp"):
        pheno_full = lax.all_gather(pheno_full, axis, axis=0, tiled=True)
    samples = pheno_full.shape[0]
    system = gram + 0.5 * samples * jnp.eye(width, dtype=jnp.float32)
    factor = jnp.linalg.cholesky(system)
    perm_part = lax.dynamic_slice_in_dim(perms, offset_rows, quarter, 1)
    pheno_part = jnp.take(pheno_full, perm_part.T, axis=0, mode="clip")
    cross_part = jnp.dot(expo_part.T, pheno_part, precision=hi)
    cross = staged_psum(cross_part)
    coefficients = chol_solve(factor, cross)
    permuted = lax.all_gather(pheno_part, "vgrp", axis=0, tiled=True)
    residuals = permuted - jnp.dot(exposures, coefficients, precision=hi)
    nperm = residuals.shape[1]
    weighted = (
        (exposures[:, :, None] * residuals[:, None, :])
        .reshape(local_rows, width * nperm)
        .astype(jnp.bfloat16)
    )
    nz, nx, nc = (lax.axis_size(a) for a in SAMP)
    variants = genotypes.shape[1]
    own_rows = variants // (nz * nx * nc)
    order = genotypes.reshape(local_rows, nz, nx, nc, own_rows).transpose(0, 3, 2, 1, 4)
    dosages = order.reshape(local_rows, variants).astype(jnp.bfloat16)
    partial = jnp.dot(dosages.T, weighted, preferred_element_type=jnp.float32)
    blocks = partial.reshape(nc, nx, nz, own_rows * width * nperm)
    blocks = lax.psum_scatter(blocks, "core", scatter_dimension=0, tiled=False)
    blocks = lax.psum_scatter(blocks, "x", scatter_dimension=0, tiled=False)
    own_scores = lax.psum_scatter(blocks, "z", scatter_dimension=0, tiled=False)
    shaped = own_scores.reshape(own_rows, width, nperm)
    return jnp.sum(shaped * shaped, axis=1) / (samples * width)


def solution(mesh):
    nv, ns = mesh.devices.shape
    fine = Mesh(mesh.devices.reshape(nv, ns // 8, 4, 2), ALL)
    return jax.shard_map(
        per_device,
        mesh=fine,
        in_specs=(P(ALL), P(SAMP, None), P(None, SAMP), P(SAMP, "vgrp")),
        out_specs=P(ALL, None),
        check_vma=False,
    )
```

```python
import jax
import jax.numpy as jnp
from jax import lax
from jax.sharding import Mesh, PartitionSpec as P

SAMP = ("z", "x", "core")
ALL = ("vgrp",) + SAMP


def chol_solve(factor, rhs):
    middle = lax.linalg.triangular_solve(factor, rhs, left_side=True, lower=True)
    return lax.linalg.triangular_solve(factor, middle, left_side=True, lower=True, transpose_a=True)


def doubling_psum(x, axes):
    for axis in axes:
        size = lax.axis_size(axis)
        step = 1
        while step < size:
            pairs = [(i, i ^ step) for i in range(size)]
            x = x + lax.ppermute(x, axis, pairs)
            step *= 2
    return x


def per_device(phenotype, exposures, perms, genotypes):
    hi = lax.Precision.HIGHEST
    nv = lax.axis_size("vgrp")
    local_rows = exposures.shape[0]
    width = exposures.shape[1]
    quarter = local_rows // nv
    offset_rows = lax.axis_index("vgrp") * quarter
    expo_part = lax.dynamic_slice_in_dim(exposures, offset_rows, quarter, 0)
    gram_part = jnp.dot(expo_part.T, expo_part, precision=hi)
    pheno_full = phenotype
    for axis in ("core", "x", "z", "vgrp"):
        pheno_full = lax.all_gather(pheno_full, axis, axis=0, tiled=True)
    samples = pheno_full.shape[0]
    perm_part = lax.dynamic_slice_in_dim(perms, offset_rows, quarter, 1)
    pheno_part = jnp.take(pheno_full, perm_part.T, axis=0, mode="clip")
    cross_part = jnp.dot(expo_part.T, pheno_part, precision=hi)
    both = doubling_psum(jnp.concatenate([gram_part, cross_part], axis=1), ("core", "x", "z", "vgrp"))
    gram, cross = both[:, :width], both[:, width:]
    system = gram + 0.5 * samples * jnp.eye(width, dtype=jnp.float32)
    factor = jnp.linalg.cholesky(system)
    coefficients = chol_solve(factor, cross)
    permuted = lax.all_gather(pheno_part, "vgrp", axis=0, tiled=True)
    residuals = permuted - jnp.dot(exposures, coefficients, precision=hi)
    nperm = residuals.shape[1]
    weighted = (
        (exposures[:, :, None] * residuals[:, None, :])
        .reshape(local_rows, width * nperm)
        .astype(jnp.bfloat16)
    )
    nz, nx, nc = (lax.axis_size(a) for a in SAMP)
    variants = genotypes.shape[1]
    own_rows = variants // (nz * nx * nc)
    order = genotypes.reshape(local_rows, nz, nx, nc, own_rows).transpose(0, 3, 2, 1, 4)
    dosages = order.reshape(local_rows, variants).astype(jnp.bfloat16)
    partial = jnp.dot(dosages.T, weighted, preferred_element_type=jnp.float32)
    blocks = partial.reshape(nc, nx, nz, own_rows * width * nperm)
    blocks = lax.psum_scatter(blocks, "core", scatter_dimension=0, tiled=False)
    blocks = lax.psum_scatter(blocks, "x", scatter_dimension=0, tiled=False)
    own_scores = jnp.sum(lax.all_to_all(blocks, "z", 0, 0, tiled=True), axis=0)
    shaped = own_scores.reshape(own_rows, width, nperm)
    return jnp.sum(shaped * shaped, axis=1) / (samples * width)


def solution(mesh):
    nv, ns = mesh.devices.shape
    fine = Mesh(mesh.devices.reshape(nv, ns // 8, 4, 2), ALL)
    return jax.shard_map(
        per_device,
        mesh=fine,
        in_specs=(P(ALL), P(SAMP, None), P(None, SAMP), P(SAMP, "vgrp")),
        out_specs=P(ALL, None),
        check_vma=False,
    )
```

```python
import jax
import jax.numpy as jnp
from jax import lax
from jax.experimental import pallas as pl
from jax.sharding import Mesh, PartitionSpec as P

SAMP = ("z", "x", "core")
ALL = ("vgrp",) + SAMP


def chol_solve(factor, rhs):
    middle = lax.linalg.triangular_solve(factor, rhs, left_side=True, lower=True)
    return lax.linalg.triangular_solve(factor, middle, left_side=True, lower=True, transpose_a=True)


COLS = 256
TILE = 512


def gather_body(idx_ref, tab_ref, out_ref):
    idx = idx_ref[...]
    rows = tab_ref.shape[1]
    row = idx // COLS
    col = idx % COLS
    hot = (lax.broadcasted_iota(jnp.int32, (rows, TILE), 0) == row).astype(jnp.bfloat16)
    picked = jnp.dot(tab_ref[...], hot, preferred_element_type=jnp.float32)
    value = picked[:COLS] + picked[COLS : 2 * COLS] + picked[2 * COLS :]
    wanted = lax.broadcasted_iota(jnp.int32, (COLS, TILE), 0) == col
    out_ref[...] = jnp.sum(jnp.where(wanted, value, jnp.float32(0.0)), axis=0, keepdims=True)


def split_table(pheno_full):
    table = pheno_full.reshape(-1, COLS)
    top = lax.reduce_precision(table, exponent_bits=8, mantissa_bits=7)
    rest = table - top
    middle = lax.reduce_precision(rest, exponent_bits=8, mantissa_bits=7)
    low = rest - middle
    pieces = [piece.T.astype(jnp.bfloat16) for piece in (top, middle, low)]
    return jnp.concatenate(pieces, axis=0)


def gather_pheno(pheno_full, index, interpret=False):
    stacked = split_table(pheno_full)
    count = index.size
    flat = index.reshape(1, count)
    out = pl.pallas_call(
        gather_body,
        grid=(count // TILE,),
        in_specs=[
            pl.BlockSpec((1, TILE), lambda i: (0, i)),
            pl.BlockSpec(stacked.shape, lambda i: (0, 0)),
        ],
        out_specs=pl.BlockSpec((1, TILE), lambda i: (0, i)),
        out_shape=jax.ShapeDtypeStruct((1, count), jnp.float32),
        interpret=interpret,
    )(flat, stacked)
    return out.reshape(index.shape)


def doubling_psum(x, axes):
    for axis in axes:
        size = lax.axis_size(axis)
        step = 1
        while step < size:
            pairs = [(i, i ^ step) for i in range(size)]
            x = x + lax.ppermute(x, axis, pairs)
            step *= 2
    return x


def per_device(phenotype, exposures, perms, genotypes):
    hi = lax.Precision.HIGHEST
    nv = lax.axis_size("vgrp")
    local_rows = exposures.shape[0]
    width = exposures.shape[1]
    quarter = local_rows // nv
    offset_rows = lax.axis_index("vgrp") * quarter
    expo_part = lax.dynamic_slice_in_dim(exposures, offset_rows, quarter, 0)
    gram_part = jnp.dot(expo_part.T, expo_part, precision=hi)
    pheno_full = phenotype
    for axis in ("core", "x", "z", "vgrp"):
        pheno_full = lax.all_gather(pheno_full, axis, axis=0, tiled=True)
    samples = pheno_full.shape[0]
    perm_part = lax.dynamic_slice_in_dim(perms, offset_rows, quarter, 1)
    pheno_part = gather_pheno(pheno_full, perm_part).T
    cross_part = jnp.dot(expo_part.T, pheno_part, precision=hi)
    both = doubling_psum(jnp.concatenate([gram_part, cross_part], axis=1), ("core", "x", "z", "vgrp"))
    gram, cross = both[:, :width], both[:, width:]
    system = gram + 0.5 * samples * jnp.eye(width, dtype=jnp.float32)
    factor = jnp.linalg.cholesky(system)
    coefficients = chol_solve(factor, cross)
    permuted = lax.all_gather(pheno_part, "vgrp", axis=0, tiled=True)
    residuals = permuted - jnp.dot(exposures, coefficients, precision=hi)
    nperm = residuals.shape[1]
    weighted = (
        (exposures[:, :, None] * residuals[:, None, :])
        .reshape(local_rows, width * nperm)
        .astype(jnp.bfloat16)
    )
    nz, nx, nc = (lax.axis_size(a) for a in SAMP)
    variants = genotypes.shape[1]
    own_rows = variants // (nz * nx * nc)
    order = genotypes.reshape(local_rows, nz, nx, nc, own_rows).transpose(0, 3, 2, 1, 4)
    dosages = order.reshape(local_rows, variants).astype(jnp.bfloat16)
    partial = jnp.dot(dosages.T, weighted, preferred_element_type=jnp.float32)
    blocks = partial.reshape(nc, nx, nz, own_rows * width * nperm)
    blocks = lax.psum_scatter(blocks, "core", scatter_dimension=0, tiled=False)
    blocks = lax.psum_scatter(blocks, "x", scatter_dimension=0, tiled=False)
    own_scores = jnp.sum(lax.all_to_all(blocks, "z", 0, 0, tiled=True), axis=0)
    shaped = own_scores.reshape(own_rows, width, nperm)
    return jnp.sum(shaped * shaped, axis=1) / (samples * width)


def solution(mesh):
    nv, ns = mesh.devices.shape
    fine = Mesh(mesh.devices.reshape(nv, ns // 8, 4, 2), ALL)
    return jax.shard_map(
        per_device,
        mesh=fine,
        in_specs=(P(ALL), P(SAMP, None), P(None, SAMP), P(SAMP, "vgrp")),
        out_specs=P(ALL, None),
        check_vma=False,
    )
```

```python
import jax
import jax.numpy as jnp
from jax import lax
from jax.experimental import pallas as pl
from jax.sharding import Mesh, PartitionSpec as P

SAMP = ("z", "x", "core")
ALL = ("vgrp",) + SAMP


def chol_solve(factor, rhs):
    middle = lax.linalg.triangular_solve(factor, rhs, left_side=True, lower=True)
    return lax.linalg.triangular_solve(factor, middle, left_side=True, lower=True, transpose_a=True)


COLS = 256
TILE = 512


def gather_body(idx_ref, tab_ref, out_ref):
    idx = idx_ref[...]
    rows = tab_ref.shape[1]
    row = idx // COLS
    col = idx % COLS
    hot = (lax.broadcasted_iota(jnp.int32, (rows, TILE), 0) == row).astype(jnp.bfloat16)
    picked = jnp.dot(tab_ref[...], hot, preferred_element_type=jnp.float32)
    value = picked[:COLS] + picked[COLS : 2 * COLS] + picked[2 * COLS :]
    wanted = lax.broadcasted_iota(jnp.int32, (COLS, TILE), 0) == col
    out_ref[...] = jnp.sum(jnp.where(wanted, value, jnp.float32(0.0)), axis=0, keepdims=True)


def split_table(pheno_full):
    table = pheno_full.reshape(-1, COLS)
    top = lax.reduce_precision(table, exponent_bits=8, mantissa_bits=7)
    rest = table - top
    middle = lax.reduce_precision(rest, exponent_bits=8, mantissa_bits=7)
    low = rest - middle
    pieces = [piece.T.astype(jnp.bfloat16) for piece in (top, middle, low)]
    return jnp.concatenate(pieces, axis=0)


def gather_pheno(pheno_full, index, interpret=False):
    stacked = split_table(pheno_full)
    count = index.size
    flat = index.reshape(1, count)
    out = pl.pallas_call(
        gather_body,
        grid=(count // TILE,),
        in_specs=[
            pl.BlockSpec((1, TILE), lambda i: (0, i)),
            pl.BlockSpec(stacked.shape, lambda i: (0, 0)),
        ],
        out_specs=pl.BlockSpec((1, TILE), lambda i: (0, i)),
        out_shape=jax.ShapeDtypeStruct((1, count), jnp.float32),
        interpret=interpret,
    )(flat, stacked)
    return out.reshape(index.shape)


def doubling_psum(x, axes):
    for axis in axes:
        size = lax.axis_size(axis)
        step = 1
        while step < size:
            pairs = [(i, i ^ step) for i in range(size)]
            x = x + lax.ppermute(x, axis, pairs)
            step *= 2
    return x


def split_bits():
    bits = []
    for axis, count in (("core", 1), ("x", 2), ("z", 3)):
        for level in range(count):
            bits.append((axis, level))
    return bits


def exchange(keep_lo, keep_hi, axis, level, along):
    size = lax.axis_size(axis)
    bit = (lax.axis_index(axis) >> level) & 1
    flip = [(i, i ^ (1 << level)) for i in range(size)]
    send = jnp.where(bit == 0, keep_hi, keep_lo)
    mine = jnp.where(bit == 0, keep_lo, keep_hi)
    return mine + lax.ppermute(send, axis, flip)


def halving_scores(weighted, genotypes):
    bits = split_bits()
    local_rows, variants = genotypes.shape
    nz, nx, nc = (lax.axis_size(a) for a in SAMP)
    own_rows = variants // (nz * nx * nc)
    order = genotypes.reshape(local_rows, 2, 2, 2, 2, 2, nc, own_rows)
    order = order.transpose(0, 6, 5, 4, 3, 2, 1, 7)
    dosages = order.reshape(local_rows, variants).astype(jnp.bfloat16)
    cur = jnp.dot(weighted.T, dosages, preferred_element_type=jnp.float32)
    for axis, level in bits[:2]:
        half = cur.shape[1] // 2
        cur = exchange(cur[:, :half], cur[:, half:], axis, level, 1)
    cur = cur.T
    for axis, level in bits[2:]:
        half = cur.shape[0] // 2
        cur = exchange(cur[:half], cur[half:], axis, level, 0)
    return cur


def per_device(phenotype, exposures, perms, genotypes):
    hi = lax.Precision.HIGHEST
    nv = lax.axis_size("vgrp")
    local_rows = exposures.shape[0]
    width = exposures.shape[1]
    quarter = local_rows // nv
    offset_rows = lax.axis_index("vgrp") * quarter
    expo_part = lax.dynamic_slice_in_dim(exposures, offset_rows, quarter, 0)
    gram_part = jnp.dot(expo_part.T, expo_part, precision=hi)
    pheno_full = phenotype
    for axis in ("core", "x", "z", "vgrp"):
        pheno_full = lax.all_gather(pheno_full, axis, axis=0, tiled=True)
    samples = pheno_full.shape[0]
    perm_part = lax.dynamic_slice_in_dim(perms, offset_rows, quarter, 1)
    pheno_part = gather_pheno(pheno_full, perm_part).T
    cross_part = jnp.dot(expo_part.T, pheno_part, precision=hi)
    both = doubling_psum(jnp.concatenate([gram_part, cross_part], axis=1), ("core", "x", "z", "vgrp"))
    gram, cross = both[:, :width], both[:, width:]
    system = gram + 0.5 * samples * jnp.eye(width, dtype=jnp.float32)
    factor = jnp.linalg.cholesky(system)
    coefficients = chol_solve(factor, cross)
    permuted = lax.all_gather(pheno_part, "vgrp", axis=0, tiled=True)
    residuals = permuted - jnp.dot(exposures, coefficients, precision=hi)
    nperm = residuals.shape[1]
    weighted = (
        (exposures[:, :, None] * residuals[:, None, :])
        .reshape(local_rows, width * nperm)
        .astype(jnp.bfloat16)
    )
    own_scores = halving_scores(weighted, genotypes)
    shaped = own_scores.reshape(own_scores.shape[0], width, nperm)
    return jnp.sum(shaped * shaped, axis=1) / (samples * width)


def solution(mesh):
    nv, ns = mesh.devices.shape
    fine = Mesh(mesh.devices.reshape(nv, ns // 8, 4, 2), ALL)
    return jax.shard_map(
        per_device,
        mesh=fine,
        in_specs=(P(ALL), P(SAMP, None), P(None, SAMP), P(SAMP, "vgrp")),
        out_specs=P(ALL, None),
        check_vma=False,
    )
```

```python
import jax
import jax.numpy as jnp
from jax import lax
from jax.experimental import pallas as pl
from jax.sharding import Mesh, PartitionSpec as P

SAMP = ("z", "x", "core")
ALL = ("vgrp",) + SAMP


def chol_solve(factor, rhs):
    middle = lax.linalg.triangular_solve(factor, rhs, left_side=True, lower=True)
    return lax.linalg.triangular_solve(factor, middle, left_side=True, lower=True, transpose_a=True)


COLS = 256
TILE = 512


def gather_body(idx_ref, tab_ref, out_ref):
    idx = idx_ref[...]
    rows = tab_ref.shape[1]
    row = idx // COLS
    col = idx % COLS
    hot = (lax.broadcasted_iota(jnp.int32, (rows, TILE), 0) == row).astype(jnp.bfloat16)
    picked = jnp.dot(tab_ref[...], hot, preferred_element_type=jnp.float32)
    value = picked[:COLS] + picked[COLS : 2 * COLS] + picked[2 * COLS :]
    wanted = lax.broadcasted_iota(jnp.int32, (COLS, TILE), 0) == col
    out_ref[...] = jnp.sum(jnp.where(wanted, value, jnp.float32(0.0)), axis=0, keepdims=True)


def split_table(pheno_full):
    table = pheno_full.reshape(-1, COLS)
    top = lax.reduce_precision(table, exponent_bits=8, mantissa_bits=7)
    rest = table - top
    middle = lax.reduce_precision(rest, exponent_bits=8, mantissa_bits=7)
    low = rest - middle
    pieces = [piece.T.astype(jnp.bfloat16) for piece in (top, middle, low)]
    return jnp.concatenate(pieces, axis=0)


def gather_pheno(pheno_full, index, interpret=False):
    stacked = split_table(pheno_full)
    count = index.size
    flat = index.reshape(1, count)
    out = pl.pallas_call(
        gather_body,
        grid=(count // TILE,),
        in_specs=[
            pl.BlockSpec((1, TILE), lambda i: (0, i)),
            pl.BlockSpec(stacked.shape, lambda i: (0, 0)),
        ],
        out_specs=pl.BlockSpec((1, TILE), lambda i: (0, i)),
        out_shape=jax.ShapeDtypeStruct((1, count), jnp.float32),
        interpret=interpret,
    )(flat, stacked)
    return out.reshape(index.shape)


def doubling_psum(x, axes):
    for axis in axes:
        size = lax.axis_size(axis)
        step = 1
        while step < size:
            pairs = [(i, i ^ step) for i in range(size)]
            x = x + lax.ppermute(x, axis, pairs)
            step *= 2
    return x


def doubling_gather(x, steps):
    for axis, level in steps:
        size = lax.axis_size(axis)
        bit = (lax.axis_index(axis) >> level) & 1
        flip = [(i, i ^ (1 << level)) for i in range(size)]
        other = lax.ppermute(x, axis, flip)
        low = jnp.where(bit == 0, x, other)
        high = jnp.where(bit == 0, other, x)
        x = jnp.concatenate([low, high], axis=0)
    return x


def axis_bits(axes):
    steps = []
    for axis in axes:
        level = 0
        while (1 << level) < lax.axis_size(axis):
            steps.append((axis, level))
            level += 1
    return steps


def split_bits():
    bits = []
    for axis, count in (("core", 1), ("x", 2), ("z", 3)):
        for level in range(count):
            bits.append((axis, level))
    return bits


def exchange(keep_lo, keep_hi, axis, level, along):
    size = lax.axis_size(axis)
    bit = (lax.axis_index(axis) >> level) & 1
    flip = [(i, i ^ (1 << level)) for i in range(size)]
    send = jnp.where(bit == 0, keep_hi, keep_lo)
    mine = jnp.where(bit == 0, keep_lo, keep_hi)
    return mine + lax.ppermute(send, axis, flip)


def halving_scores(weighted, genotypes):
    bits = split_bits()
    local_rows, variants = genotypes.shape
    nz, nx, nc = (lax.axis_size(a) for a in SAMP)
    own_rows = variants // (nz * nx * nc)
    order = genotypes.reshape(local_rows, 2, 2, 2, 2, 2, nc, own_rows)
    order = order.transpose(0, 6, 5, 4, 3, 2, 1, 7)
    dosages = order.reshape(local_rows, variants).astype(jnp.bfloat16)
    cur = jnp.dot(weighted.T, dosages, preferred_element_type=jnp.float32)
    for axis, level in bits[:2]:
        half = cur.shape[1] // 2
        cur = exchange(cur[:, :half], cur[:, half:], axis, level, 1)
    cur = cur.T
    for axis, level in bits[2:]:
        half = cur.shape[0] // 2
        cur = exchange(cur[:half], cur[half:], axis, level, 0)
    return cur


def per_device(phenotype, exposures, perms, genotypes):
    hi = lax.Precision.HIGHEST
    nv = lax.axis_size("vgrp")
    local_rows = exposures.shape[0]
    width = exposures.shape[1]
    quarter = local_rows // nv
    offset_rows = lax.axis_index("vgrp") * quarter
    expo_part = lax.dynamic_slice_in_dim(exposures, offset_rows, quarter, 0)
    gram_part = jnp.dot(expo_part.T, expo_part, precision=hi)
    gram = doubling_psum(gram_part, ("core", "x", "z", "vgrp"))
    pheno_full = doubling_gather(phenotype, axis_bits(("core", "x", "z", "vgrp")))
    samples = pheno_full.shape[0]
    system = gram + 0.5 * samples * jnp.eye(width, dtype=jnp.float32)
    factor = jnp.linalg.cholesky(system)
    perm_part = lax.dynamic_slice_in_dim(perms, offset_rows, quarter, 1)
    pheno_part = gather_pheno(pheno_full, perm_part).T
    cross_part = jnp.dot(expo_part.T, pheno_part, precision=hi)
    cross = doubling_psum(cross_part, ("core", "x", "z", "vgrp"))
    coefficients = chol_solve(factor, cross)
    permuted = doubling_gather(pheno_part, axis_bits(("vgrp",)))
    residuals = permuted - jnp.dot(exposures, coefficients, precision=hi)
    nperm = residuals.shape[1]
    weighted = (
        (exposures[:, :, None] * residuals[:, None, :])
        .reshape(local_rows, width * nperm)
        .astype(jnp.bfloat16)
    )
    own_scores = halving_scores(weighted, genotypes)
    shaped = own_scores.reshape(own_scores.shape[0], width, nperm)
    return jnp.sum(shaped * shaped, axis=1) / (samples * width)


def solution(mesh):
    nv, ns = mesh.devices.shape
    fine = Mesh(mesh.devices.reshape(nv, ns // 8, 4, 2), ALL)
    return jax.shard_map(
        per_device,
        mesh=fine,
        in_specs=(P(ALL), P(SAMP, None), P(None, SAMP), P(SAMP, "vgrp")),
        out_specs=P(ALL, None),
        check_vma=False,
    )
```

```python
import jax
import jax.numpy as jnp
from jax import lax
from jax.experimental import pallas as pl
from jax.sharding import Mesh, PartitionSpec as P

SAMP = ("z", "x", "core")
ALL = ("vgrp",) + SAMP


def chol_solve(factor, rhs):
    middle = lax.linalg.triangular_solve(factor, rhs, left_side=True, lower=True)
    return lax.linalg.triangular_solve(factor, middle, left_side=True, lower=True, transpose_a=True)


COLS = 256
TILE = 512


def gather_body(idx_ref, tab_ref, out_ref):
    idx = idx_ref[...]
    rows = tab_ref.shape[1]
    row = idx // COLS
    col = idx % COLS
    hot = (lax.broadcasted_iota(jnp.int32, (rows, TILE), 0) == row).astype(jnp.bfloat16)
    picked = jnp.dot(tab_ref[...], hot, preferred_element_type=jnp.float32)
    value = picked[:COLS] + picked[COLS : 2 * COLS] + picked[2 * COLS :]
    wanted = lax.broadcasted_iota(jnp.int32, (COLS, TILE), 0) == col
    out_ref[...] = jnp.sum(jnp.where(wanted, value, jnp.float32(0.0)), axis=0, keepdims=True)


def split_table(pheno_full):
    table = pheno_full.reshape(-1, COLS)
    top = lax.reduce_precision(table, exponent_bits=8, mantissa_bits=7)
    rest = table - top
    middle = lax.reduce_precision(rest, exponent_bits=8, mantissa_bits=7)
    low = rest - middle
    pieces = [piece.T.astype(jnp.bfloat16) for piece in (top, middle, low)]
    return jnp.concatenate(pieces, axis=0)


def gather_pheno(pheno_full, index, interpret=False):
    stacked = split_table(pheno_full)
    count = index.size
    flat = index.reshape(1, count)
    out = pl.pallas_call(
        gather_body,
        grid=(count // TILE,),
        in_specs=[
            pl.BlockSpec((1, TILE), lambda i: (0, i)),
            pl.BlockSpec(stacked.shape, lambda i: (0, 0)),
        ],
        out_specs=pl.BlockSpec((1, TILE), lambda i: (0, i)),
        out_shape=jax.ShapeDtypeStruct((1, count), jnp.float32),
        interpret=interpret,
    )(flat, stacked)
    return out.reshape(index.shape)


def doubling_psum(x, axes):
    for axis in axes:
        size = lax.axis_size(axis)
        step = 1
        while step < size:
            pairs = [(i, i ^ step) for i in range(size)]
            x = x + lax.ppermute(x, axis, pairs)
            step *= 2
    return x


def doubling_gather(x, steps):
    for axis, level in steps:
        size = lax.axis_size(axis)
        bit = (lax.axis_index(axis) >> level) & 1
        flip = [(i, i ^ (1 << level)) for i in range(size)]
        other = lax.ppermute(x, axis, flip)
        low = jnp.where(bit == 0, x, other)
        high = jnp.where(bit == 0, other, x)
        x = jnp.concatenate([low, high], axis=0)
    return x


def axis_bits(axes):
    steps = []
    for axis in axes:
        level = 0
        while (1 << level) < lax.axis_size(axis):
            steps.append((axis, level))
            level += 1
    return steps


def split_bits():
    bits = []
    for axis, count in (("core", 1), ("x", 2), ("z", 3)):
        for level in range(count):
            bits.append((axis, level))
    return bits


def exchange(keep_lo, keep_hi, axis, level, along):
    size = lax.axis_size(axis)
    bit = (lax.axis_index(axis) >> level) & 1
    flip = [(i, i ^ (1 << level)) for i in range(size)]
    send = jnp.where(bit == 0, keep_hi, keep_lo)
    mine = jnp.where(bit == 0, keep_lo, keep_hi)
    return mine + lax.ppermute(send, axis, flip)


def halve_bit(cur, names, name):
    position = len(names) - 1 - names.index(name) + 3
    rows, cols = cur.shape
    axis, level = name
    size = lax.axis_size(axis)
    bit = (lax.axis_index(axis) >> level) & 1
    flip = [(i, i ^ (1 << level)) for i in range(size)]
    split = cur.reshape(rows >> (position + 1), 2, 1 << position, cols)
    low, high = split[:, 0], split[:, 1]
    send = jnp.where(bit == 0, high, low)
    mine = jnp.where(bit == 0, low, high)
    kept = mine + lax.ppermute(send, axis, flip)
    return kept.reshape(rows // 2, cols), [n for n in names if n != name]


def halving_scores(weighted, genotypes):
    local_rows, variants = genotypes.shape
    nz, nx, nc = (lax.axis_size(a) for a in SAMP)
    own_rows = variants // (nz * nx * nc)
    order = genotypes.reshape(local_rows, 2, 2, 2, 2, 2, nc, own_rows)
    order = order.transpose(0, 6, 5, 4, 3, 2, 1, 7)
    dosages = order.reshape(local_rows, variants).astype(jnp.bfloat16)
    cur = jnp.dot(weighted.T, dosages, preferred_element_type=jnp.float32)
    half = cur.shape[1] // 2
    cur = exchange(cur[:, :half], cur[:, half:], "core", 0, 1).T
    names = [("x", 0), ("x", 1), ("z", 0), ("z", 1), ("z", 2)]
    cols = cur.shape[1] // 2
    part_a, names_a = cur[:, :cols], list(names)
    part_b, names_b = cur[:, cols:], list(names)
    plan = [(("x", 0), ("z", 0)), (("z", 0), ("x", 0)), (("x", 1), ("z", 1)), (("z", 1), ("x", 1))]
    for step_a, step_b in plan:
        part_a, names_a = halve_bit(part_a, names_a, step_a)
        part_b, names_b = halve_bit(part_b, names_b, step_b)
    cur = jnp.concatenate([part_a, part_b], axis=1)
    cur, _ = halve_bit(cur, names_a, ("z", 2))
    return cur


def per_device(phenotype, exposures, perms, genotypes):
    hi = lax.Precision.HIGHEST
    nv = lax.axis_size("vgrp")
    local_rows = exposures.shape[0]
    width = exposures.shape[1]
    quarter = local_rows // nv
    offset_rows = lax.axis_index("vgrp") * quarter
    expo_part = lax.dynamic_slice_in_dim(exposures, offset_rows, quarter, 0)
    gram_part = jnp.dot(expo_part.T, expo_part, precision=hi)
    gram = doubling_psum(gram_part, ("core", "x", "z", "vgrp"))
    pheno_full = doubling_gather(phenotype, axis_bits(("core", "x", "z", "vgrp")))
    samples = pheno_full.shape[0]
    system = gram + 0.5 * samples * jnp.eye(width, dtype=jnp.float32)
    factor = jnp.linalg.cholesky(system)
    perm_part = lax.dynamic_slice_in_dim(perms, offset_rows, quarter, 1)
    pheno_part = gather_pheno(pheno_full, perm_part).T
    cross_part = jnp.dot(expo_part.T, pheno_part, precision=hi)
    cross = doubling_psum(cross_part, ("core", "x", "z", "vgrp"))
    coefficients = chol_solve(factor, cross)
    permuted = doubling_gather(pheno_part, axis_bits(("vgrp",)))
    residuals = permuted - jnp.dot(exposures, coefficients, precision=hi)
    nperm = residuals.shape[1]
    weighted = (
        (exposures[:, :, None] * residuals[:, None, :])
        .reshape(local_rows, width * nperm)
        .astype(jnp.bfloat16)
    )
    own_scores = halving_scores(weighted, genotypes)
    shaped = own_scores.reshape(own_scores.shape[0], width, nperm)
    return jnp.sum(shaped * shaped, axis=1) / (samples * width)


def solution(mesh):
    nv, ns = mesh.devices.shape
    fine = Mesh(mesh.devices.reshape(nv, ns // 8, 4, 2), ALL)
    return jax.shard_map(
        per_device,
        mesh=fine,
        in_specs=(P(ALL), P(SAMP, None), P(None, SAMP), P(SAMP, "vgrp")),
        out_specs=P(ALL, None),
        check_vma=False,
    )
```

```python
import jax
import jax.numpy as jnp
from jax import lax
from jax.experimental import pallas as pl
from jax.sharding import Mesh, PartitionSpec as P

SAMP = ("z", "x", "core")
ALL = ("vgrp",) + SAMP


def chol_solve(factor, rhs):
    middle = lax.linalg.triangular_solve(factor, rhs, left_side=True, lower=True)
    return lax.linalg.triangular_solve(factor, middle, left_side=True, lower=True, transpose_a=True)


COLS = 256
TILE = 512


def gather_body(idx_ref, tab_ref, out_ref):
    idx = idx_ref[...]
    rows = tab_ref.shape[1]
    row = idx // COLS
    col = idx % COLS
    hot = (lax.broadcasted_iota(jnp.int32, (rows, TILE), 0) == row).astype(jnp.bfloat16)
    picked = jnp.dot(tab_ref[...], hot, preferred_element_type=jnp.float32)
    value = picked[:COLS] + picked[COLS : 2 * COLS] + picked[2 * COLS :]
    wanted = lax.broadcasted_iota(jnp.int32, (COLS, TILE), 0) == col
    out_ref[...] = jnp.sum(jnp.where(wanted, value, jnp.float32(0.0)), axis=0, keepdims=True)


def split_table(pheno_full):
    table = pheno_full.reshape(-1, COLS)
    top = lax.reduce_precision(table, exponent_bits=8, mantissa_bits=7)
    rest = table - top
    middle = lax.reduce_precision(rest, exponent_bits=8, mantissa_bits=7)
    low = rest - middle
    pieces = [piece.T.astype(jnp.bfloat16) for piece in (top, middle, low)]
    return jnp.concatenate(pieces, axis=0)


def gather_pheno(pheno_full, index, interpret=False):
    stacked = split_table(pheno_full)
    count = index.size
    flat = index.reshape(1, count)
    out = pl.pallas_call(
        gather_body,
        grid=(count // TILE,),
        in_specs=[
            pl.BlockSpec((1, TILE), lambda i: (0, i)),
            pl.BlockSpec(stacked.shape, lambda i: (0, 0)),
        ],
        out_specs=pl.BlockSpec((1, TILE), lambda i: (0, i)),
        out_shape=jax.ShapeDtypeStruct((1, count), jnp.float32),
        interpret=interpret,
    )(flat, stacked)
    return out.reshape(index.shape)


def doubling_psum(x, axes):
    for axis in axes:
        size = lax.axis_size(axis)
        step = 1
        while step < size:
            pairs = [(i, i ^ step) for i in range(size)]
            x = x + lax.ppermute(x, axis, pairs)
            step *= 2
    return x


def doubling_gather(x, steps):
    for axis, level in steps:
        size = lax.axis_size(axis)
        bit = (lax.axis_index(axis) >> level) & 1
        flip = [(i, i ^ (1 << level)) for i in range(size)]
        other = lax.ppermute(x, axis, flip)
        low = jnp.where(bit == 0, x, other)
        high = jnp.where(bit == 0, other, x)
        x = jnp.concatenate([low, high], axis=0)
    return x


def axis_bits(axes):
    steps = []
    for axis in axes:
        level = 0
        while (1 << level) < lax.axis_size(axis):
            steps.append((axis, level))
            level += 1
    return steps


def split_bits():
    bits = []
    for axis, count in (("core", 1), ("x", 2), ("z", 3)):
        for level in range(count):
            bits.append((axis, level))
    return bits


def exchange(keep_lo, keep_hi, axis, level, along):
    size = lax.axis_size(axis)
    bit = (lax.axis_index(axis) >> level) & 1
    flip = [(i, i ^ (1 << level)) for i in range(size)]
    send = jnp.where(bit == 0, keep_hi, keep_lo)
    mine = jnp.where(bit == 0, keep_lo, keep_hi)
    return mine + lax.ppermute(send, axis, flip)


def halve_bit(cur, names, name):
    position = len(names) - 1 - names.index(name) + 3
    rows, cols = cur.shape
    axis, level = name
    size = lax.axis_size(axis)
    bit = (lax.axis_index(axis) >> level) & 1
    flip = [(i, i ^ (1 << level)) for i in range(size)]
    split = cur.reshape(rows >> (position + 1), 2, 1 << position, cols)
    low, high = split[:, 0], split[:, 1]
    send = jnp.where(bit == 0, high, low)
    mine = jnp.where(bit == 0, low, high)
    kept = mine + lax.ppermute(send, axis, flip)
    return kept.reshape(rows // 2, cols), [n for n in names if n != name]


def halving_scores(weighted, genotypes):
    dosages = genotypes.astype(jnp.bfloat16)
    cur = jnp.dot(weighted.T, dosages, preferred_element_type=jnp.float32).T
    names = [("z", 2), ("z", 1), ("z", 0), ("x", 1), ("x", 0), ("core", 0)]
    cur, names = halve_bit(cur, names, ("core", 0))
    cols = cur.shape[1] // 2
    part_a, names_a = cur[:, :cols], list(names)
    part_b, names_b = cur[:, cols:], list(names)
    plan = [(("x", 0), ("z", 0)), (("z", 0), ("x", 0)), (("x", 1), ("z", 1)), (("z", 1), ("x", 1))]
    for step_a, step_b in plan:
        part_a, names_a = halve_bit(part_a, names_a, step_a)
        part_b, names_b = halve_bit(part_b, names_b, step_b)
    cur = jnp.concatenate([part_a, part_b], axis=1)
    cur, _ = halve_bit(cur, names_a, ("z", 2))
    return cur


def per_device(phenotype, exposures, perms, genotypes):
    hi = lax.Precision.HIGHEST
    nv = lax.axis_size("vgrp")
    local_rows = exposures.shape[0]
    width = exposures.shape[1]
    quarter = local_rows // nv
    offset_rows = lax.axis_index("vgrp") * quarter
    expo_part = lax.dynamic_slice_in_dim(exposures, offset_rows, quarter, 0)
    gram_part = jnp.dot(expo_part.T, expo_part, precision=hi)
    gram = doubling_psum(gram_part, ("core", "x", "z", "vgrp"))
    pheno_full = doubling_gather(phenotype, axis_bits(("core", "x", "z", "vgrp")))
    samples = pheno_full.shape[0]
    system = gram + 0.5 * samples * jnp.eye(width, dtype=jnp.float32)
    factor = jnp.linalg.cholesky(system)
    inverse = chol_solve(factor, jnp.eye(width, dtype=jnp.float32))
    perm_part = lax.dynamic_slice_in_dim(perms, offset_rows, quarter, 1)
    pheno_part = gather_pheno(pheno_full, perm_part).T
    cross_part = jnp.dot(expo_part.T, pheno_part, precision=hi)
    cross = doubling_psum(cross_part, ("core", "x", "z", "vgrp"))
    coefficients = jnp.dot(inverse, cross, precision=hi)
    permuted = doubling_gather(pheno_part, axis_bits(("vgrp",)))
    residuals = permuted - jnp.dot(exposures, coefficients, precision=hi)
    nperm = residuals.shape[1]
    weighted = (
        (exposures[:, :, None] * residuals[:, None, :])
        .reshape(local_rows, width * nperm)
        .astype(jnp.bfloat16)
    )
    own_scores = halving_scores(weighted, genotypes)
    shaped = own_scores.reshape(own_scores.shape[0], width, nperm)
    return jnp.sum(shaped * shaped, axis=1) / (samples * width)


def solution(mesh):
    nv, ns = mesh.devices.shape
    fine = Mesh(mesh.devices.reshape(nv, ns // 8, 4, 2), ALL)
    return jax.shard_map(
        per_device,
        mesh=fine,
        in_specs=(P(ALL), P(SAMP, None), P(None, SAMP), P(SAMP, "vgrp")),
        out_specs=P(ALL, None),
        check_vma=False,
    )
```

```python
import jax
import jax.numpy as jnp
from jax import lax
from jax.experimental import pallas as pl
from jax.sharding import Mesh, PartitionSpec as P

SAMP = ("z", "x", "core")
ALL = ("vgrp",) + SAMP


def chol_solve(factor, rhs):
    middle = lax.linalg.triangular_solve(factor, rhs, left_side=True, lower=True)
    return lax.linalg.triangular_solve(factor, middle, left_side=True, lower=True, transpose_a=True)


COLS = 256
TILE = 512


def gather_body(idx_ref, tab_ref, out_ref):
    idx = idx_ref[...]
    rows = tab_ref.shape[1]
    row = idx // COLS
    col = idx % COLS
    hot = (lax.broadcasted_iota(jnp.int32, (rows, TILE), 0) == row).astype(jnp.bfloat16)
    picked = jnp.dot(tab_ref[...], hot, preferred_element_type=jnp.float32)
    value = picked[:COLS] + picked[COLS : 2 * COLS] + picked[2 * COLS :]
    wanted = lax.broadcasted_iota(jnp.int32, (COLS, TILE), 0) == col
    out_ref[...] = jnp.sum(jnp.where(wanted, value, jnp.float32(0.0)), axis=0, keepdims=True)


def split_table(pheno_full):
    table = pheno_full.reshape(-1, COLS)
    top = lax.reduce_precision(table, exponent_bits=8, mantissa_bits=7)
    rest = table - top
    middle = lax.reduce_precision(rest, exponent_bits=8, mantissa_bits=7)
    low = rest - middle
    pieces = [piece.T.astype(jnp.bfloat16) for piece in (top, middle, low)]
    return jnp.concatenate(pieces, axis=0)


def gather_pheno(pheno_full, index, interpret=False):
    stacked = split_table(pheno_full)
    count = index.size
    flat = index.reshape(1, count)
    out = pl.pallas_call(
        gather_body,
        grid=(count // TILE,),
        in_specs=[
            pl.BlockSpec((1, TILE), lambda i: (0, i)),
            pl.BlockSpec(stacked.shape, lambda i: (0, 0)),
        ],
        out_specs=pl.BlockSpec((1, TILE), lambda i: (0, i)),
        out_shape=jax.ShapeDtypeStruct((1, count), jnp.float32),
        interpret=interpret,
    )(flat, stacked)
    return out.reshape(index.shape)


def doubling_psum(x, axes):
    for axis in axes:
        size = lax.axis_size(axis)
        step = 1
        while step < size:
            pairs = [(i, i ^ step) for i in range(size)]
            x = x + lax.ppermute(x, axis, pairs)
            step *= 2
    return x


def doubling_gather(x, steps):
    for axis, level in steps:
        size = lax.axis_size(axis)
        bit = (lax.axis_index(axis) >> level) & 1
        flip = [(i, i ^ (1 << level)) for i in range(size)]
        other = lax.ppermute(x, axis, flip)
        low = jnp.where(bit == 0, x, other)
        high = jnp.where(bit == 0, other, x)
        x = jnp.concatenate([low, high], axis=0)
    return x


def front_chain(pheno, gram, steps):
    for axis, level in steps:
        size = lax.axis_size(axis)
        bit = (lax.axis_index(axis) >> level) & 1
        flip = [(i, i ^ (1 << level)) for i in range(size)]
        count = pheno.shape[0]
        packed = lax.ppermute(jnp.concatenate([pheno, gram.reshape(-1)]), axis, flip)
        other, other_gram = packed[:count], packed[count:].reshape(gram.shape)
        low = jnp.where(bit == 0, pheno, other)
        high = jnp.where(bit == 0, other, pheno)
        pheno = jnp.concatenate([low, high], axis=0)
        gram = gram + other_gram
    return pheno, gram


def axis_bits(axes):
    steps = []
    for axis in axes:
        level = 0
        while (1 << level) < lax.axis_size(axis):
            steps.append((axis, level))
            level += 1
    return steps


def split_bits():
    bits = []
    for axis, count in (("core", 1), ("x", 2), ("z", 3)):
        for level in range(count):
            bits.append((axis, level))
    return bits


def exchange(keep_lo, keep_hi, axis, level, along):
    size = lax.axis_size(axis)
    bit = (lax.axis_index(axis) >> level) & 1
    flip = [(i, i ^ (1 << level)) for i in range(size)]
    send = jnp.where(bit == 0, keep_hi, keep_lo)
    mine = jnp.where(bit == 0, keep_lo, keep_hi)
    return mine + lax.ppermute(send, axis, flip)


def halve_bit(cur, names, name):
    position = len(names) - 1 - names.index(name) + 3
    rows, cols = cur.shape
    axis, level = name
    size = lax.axis_size(axis)
    bit = (lax.axis_index(axis) >> level) & 1
    flip = [(i, i ^ (1 << level)) for i in range(size)]
    split = cur.reshape(rows >> (position + 1), 2, 1 << position, cols)
    low, high = split[:, 0], split[:, 1]
    send = jnp.where(bit == 0, high, low)
    mine = jnp.where(bit == 0, low, high)
    kept = mine + lax.ppermute(send, axis, flip)
    return kept.reshape(rows // 2, cols), [n for n in names if n != name]


def halving_scores(weighted, genotypes):
    local_rows, variants = genotypes.shape
    nz, nx, nc = (lax.axis_size(a) for a in SAMP)
    own_rows = variants // (nz * nx * nc)
    order = genotypes.reshape(local_rows, 2, 2, 2, 2, 2, nc, own_rows)
    order = order.transpose(0, 6, 5, 4, 3, 2, 1, 7)
    dosages = order.reshape(local_rows, variants).astype(jnp.bfloat16)
    cur = jnp.dot(weighted.T, dosages, preferred_element_type=jnp.float32)
    half = cur.shape[1] // 2
    cur = exchange(cur[:, :half], cur[:, half:], "core", 0, 1).T
    names = [("x", 0), ("x", 1), ("z", 0), ("z", 1), ("z", 2)]
    cols = cur.shape[1] // 2
    part_a, names_a = cur[:, :cols], list(names)
    part_b, names_b = cur[:, cols:], list(names)
    plan = [(("x", 0), ("z", 0)), (("z", 0), ("x", 0)), (("x", 1), ("z", 1)), (("z", 1), ("x", 1))]
    for step_a, step_b in plan:
        part_a, names_a = halve_bit(part_a, names_a, step_a)
        part_b, names_b = halve_bit(part_b, names_b, step_b)
    cur = jnp.concatenate([part_a, part_b], axis=1)
    cur, _ = halve_bit(cur, names_a, ("z", 2))
    return cur


def per_device(phenotype, exposures, perms, genotypes):
    hi = lax.Precision.HIGHEST
    nv = lax.axis_size("vgrp")
    local_rows = exposures.shape[0]
    width = exposures.shape[1]
    quarter = local_rows // nv
    offset_rows = lax.axis_index("vgrp") * quarter
    expo_part = lax.dynamic_slice_in_dim(exposures, offset_rows, quarter, 0)
    gram_part = jnp.dot(expo_part.T, expo_part, precision=hi)
    pheno_full, gram = front_chain(phenotype, gram_part, axis_bits(("core", "x", "z", "vgrp")))
    samples = pheno_full.shape[0]
    system = gram + 0.5 * samples * jnp.eye(width, dtype=jnp.float32)
    factor = jnp.linalg.cholesky(system)
    perm_part = lax.dynamic_slice_in_dim(perms, offset_rows, quarter, 1)
    pheno_part = gather_pheno(pheno_full, perm_part).T
    cross_part = jnp.dot(expo_part.T, pheno_part, precision=hi)
    cross = doubling_psum(cross_part, ("core", "x", "z", "vgrp"))
    coefficients = chol_solve(factor, cross)
    permuted = doubling_gather(pheno_part, axis_bits(("vgrp",)))
    residuals = permuted - jnp.dot(exposures, coefficients, precision=hi)
    nperm = residuals.shape[1]
    weighted = (
        (exposures[:, :, None] * residuals[:, None, :])
        .reshape(local_rows, width * nperm)
        .astype(jnp.bfloat16)
    )
    own_scores = halving_scores(weighted, genotypes)
    shaped = own_scores.reshape(own_scores.shape[0], width, nperm)
    return jnp.sum(shaped * shaped, axis=1) / (samples * width)


def solution(mesh):
    nv, ns = mesh.devices.shape
    fine = Mesh(mesh.devices.reshape(nv, ns // 8, 4, 2), ALL)
    return jax.shard_map(
        per_device,
        mesh=fine,
        in_specs=(P(ALL), P(SAMP, None), P(None, SAMP), P(SAMP, "vgrp")),
        out_specs=P(ALL, None),
        check_vma=False,
    )
```

```python
import jax
import jax.numpy as jnp
from jax import lax
from jax.experimental import pallas as pl
from jax.sharding import Mesh, PartitionSpec as P

SAMP = ("z", "x", "core")
ALL = ("vgrp",) + SAMP


def chol_solve(factor, rhs):
    middle = lax.linalg.triangular_solve(factor, rhs, left_side=True, lower=True)
    return lax.linalg.triangular_solve(factor, middle, left_side=True, lower=True, transpose_a=True)


COLS = 256
TILE = 512


def gather_body(idx_ref, tab_ref, out_ref):
    idx = idx_ref[...]
    rows = tab_ref.shape[1]
    row = idx // COLS
    col = idx % COLS
    hot = (lax.broadcasted_iota(jnp.int32, (rows, TILE), 0) == row).astype(jnp.bfloat16)
    picked = jnp.dot(tab_ref[...], hot, preferred_element_type=jnp.float32)
    value = picked[:COLS] + picked[COLS : 2 * COLS] + picked[2 * COLS :]
    wanted = lax.broadcasted_iota(jnp.int32, (COLS, TILE), 0) == col
    out_ref[...] = jnp.sum(jnp.where(wanted, value, jnp.float32(0.0)), axis=0, keepdims=True)


def split_table(pheno_full):
    table = pheno_full.reshape(-1, COLS)
    top = lax.reduce_precision(table, exponent_bits=8, mantissa_bits=7)
    rest = table - top
    middle = lax.reduce_precision(rest, exponent_bits=8, mantissa_bits=7)
    low = rest - middle
    pieces = [piece.T.astype(jnp.bfloat16) for piece in (top, middle, low)]
    return jnp.concatenate(pieces, axis=0)


def gather_pheno(pheno_full, index, interpret=False):
    stacked = split_table(pheno_full)
    count = index.size
    flat = index.reshape(1, count)
    out = pl.pallas_call(
        gather_body,
        grid=(count // TILE,),
        in_specs=[
            pl.BlockSpec((1, TILE), lambda i: (0, i)),
            pl.BlockSpec(stacked.shape, lambda i: (0, 0)),
        ],
        out_specs=pl.BlockSpec((1, TILE), lambda i: (0, i)),
        out_shape=jax.ShapeDtypeStruct((1, count), jnp.float32),
        interpret=interpret,
    )(flat, stacked)
    return out.reshape(index.shape)


def doubling_psum(x, axes):
    for axis in axes:
        size = lax.axis_size(axis)
        step = 1
        while step < size:
            pairs = [(i, i ^ step) for i in range(size)]
            x = x + lax.ppermute(x, axis, pairs)
            step *= 2
    return x


def doubling_gather(x, steps):
    for axis, level in steps:
        size = lax.axis_size(axis)
        bit = (lax.axis_index(axis) >> level) & 1
        flip = [(i, i ^ (1 << level)) for i in range(size)]
        other = lax.ppermute(x, axis, flip)
        low = jnp.where(bit == 0, x, other)
        high = jnp.where(bit == 0, other, x)
        x = jnp.concatenate([low, high], axis=0)
    return x


def front_chain(pheno, gram, steps, side, tie_after):
    for index, (axis, level) in enumerate(steps):
        if index == tie_after:
            pheno, gram, side = lax.optimization_barrier((pheno, gram, side))
        size = lax.axis_size(axis)
        bit = (lax.axis_index(axis) >> level) & 1
        flip = [(i, i ^ (1 << level)) for i in range(size)]
        count = pheno.shape[0]
        packed = lax.ppermute(jnp.concatenate([pheno, gram.reshape(-1)]), axis, flip)
        other, other_gram = packed[:count], packed[count:].reshape(gram.shape)
        low = jnp.where(bit == 0, pheno, other)
        high = jnp.where(bit == 0, other, pheno)
        pheno = jnp.concatenate([low, high], axis=0)
        gram = gram + other_gram
    return pheno, gram, side


def axis_bits(axes):
    steps = []
    for axis in axes:
        level = 0
        while (1 << level) < lax.axis_size(axis):
            steps.append((axis, level))
            level += 1
    return steps


def split_bits():
    bits = []
    for axis, count in (("core", 1), ("x", 2), ("z", 3)):
        for level in range(count):
            bits.append((axis, level))
    return bits


def exchange(keep_lo, keep_hi, axis, level, along):
    size = lax.axis_size(axis)
    bit = (lax.axis_index(axis) >> level) & 1
    flip = [(i, i ^ (1 << level)) for i in range(size)]
    send = jnp.where(bit == 0, keep_hi, keep_lo)
    mine = jnp.where(bit == 0, keep_lo, keep_hi)
    return mine + lax.ppermute(send, axis, flip)


def halve_bit(cur, names, name):
    position = len(names) - 1 - names.index(name) + 3
    rows, cols = cur.shape
    axis, level = name
    size = lax.axis_size(axis)
    bit = (lax.axis_index(axis) >> level) & 1
    flip = [(i, i ^ (1 << level)) for i in range(size)]
    split = cur.reshape(rows >> (position + 1), 2, 1 << position, cols)
    low, high = split[:, 0], split[:, 1]
    send = jnp.where(bit == 0, high, low)
    mine = jnp.where(bit == 0, low, high)
    kept = mine + lax.ppermute(send, axis, flip)
    return kept.reshape(rows // 2, cols), [n for n in names if n != name]


def reorder_dosages(genotypes):
    local_rows, variants = genotypes.shape
    nz, nx, nc = (lax.axis_size(a) for a in SAMP)
    own_rows = variants // (nz * nx * nc)
    order = genotypes.reshape(local_rows, 2, 2, 2, 2, 2, nc, own_rows)
    order = order.transpose(0, 6, 5, 4, 3, 2, 1, 7)
    return order.reshape(local_rows, variants).astype(jnp.bfloat16)


def halving_scores(weighted, dosages):
    cur = jnp.dot(weighted.T, dosages, preferred_element_type=jnp.float32)
    half = cur.shape[1] // 2
    cur = exchange(cur[:, :half], cur[:, half:], "core", 0, 1).T
    names = [("x", 0), ("x", 1), ("z", 0), ("z", 1), ("z", 2)]
    cols = cur.shape[1] // 2
    part_a, names_a = cur[:, :cols], list(names)
    part_b, names_b = cur[:, cols:], list(names)
    plan = [(("x", 0), ("z", 0)), (("z", 0), ("x", 0)), (("x", 1), ("z", 1)), (("z", 1), ("x", 1))]
    for step_a, step_b in plan:
        part_a, names_a = halve_bit(part_a, names_a, step_a)
        part_b, names_b = halve_bit(part_b, names_b, step_b)
    cur = jnp.concatenate([part_a, part_b], axis=1)
    cur, _ = halve_bit(cur, names_a, ("z", 2))
    return cur


def per_device(phenotype, exposures, perms, genotypes):
    hi = lax.Precision.HIGHEST
    nv = lax.axis_size("vgrp")
    local_rows = exposures.shape[0]
    width = exposures.shape[1]
    quarter = local_rows // nv
    offset_rows = lax.axis_index("vgrp") * quarter
    expo_part = lax.dynamic_slice_in_dim(exposures, offset_rows, quarter, 0)
    gram_part = jnp.dot(expo_part.T, expo_part, precision=hi)
    steps = axis_bits(("core", "x", "z", "vgrp"))
    pheno_full, gram, dosages = front_chain(phenotype, gram_part, steps, reorder_dosages(genotypes), 5)
    samples = pheno_full.shape[0]
    system = gram + 0.5 * samples * jnp.eye(width, dtype=jnp.float32)
    factor = jnp.linalg.cholesky(system)
    perm_part = lax.dynamic_slice_in_dim(perms, offset_rows, quarter, 1)
    pheno_part = gather_pheno(pheno_full, perm_part).T
    cross_part = jnp.dot(expo_part.T, pheno_part, precision=hi)
    cross = doubling_psum(cross_part, ("core", "x", "z", "vgrp"))
    coefficients = chol_solve(factor, cross)
    permuted = doubling_gather(pheno_part, axis_bits(("vgrp",)))
    residuals = permuted - jnp.dot(exposures, coefficients, precision=hi)
    nperm = residuals.shape[1]
    weighted = (
        (exposures[:, :, None] * residuals[:, None, :])
        .reshape(local_rows, width * nperm)
        .astype(jnp.bfloat16)
    )
    own_scores = halving_scores(weighted, dosages)
    shaped = own_scores.reshape(own_scores.shape[0], width, nperm)
    return jnp.sum(shaped * shaped, axis=1) / (samples * width)


def solution(mesh):
    nv, ns = mesh.devices.shape
    fine = Mesh(mesh.devices.reshape(nv, ns // 8, 4, 2), ALL)
    return jax.shard_map(
        per_device,
        mesh=fine,
        in_specs=(P(ALL), P(SAMP, None), P(None, SAMP), P(SAMP, "vgrp")),
        out_specs=P(ALL, None),
        check_vma=False,
    )
```

```python
import jax
import jax.numpy as jnp
from jax import lax
from jax.experimental import pallas as pl
from jax.sharding import Mesh, PartitionSpec as P

SAMP = ("z", "x", "core")
ALL = ("vgrp",) + SAMP


def chol_solve(factor, rhs):
    middle = lax.linalg.triangular_solve(factor, rhs, left_side=True, lower=True)
    return lax.linalg.triangular_solve(factor, middle, left_side=True, lower=True, transpose_a=True)


COLS = 256
TILE = 1024


def gather_body(idx_ref, tab_ref, out_ref):
    idx = idx_ref[...]
    rows = tab_ref.shape[1]
    row = idx // COLS
    col = idx % COLS
    hot = (lax.broadcasted_iota(jnp.int32, (rows, TILE), 0) == row).astype(jnp.bfloat16)
    picked = jnp.dot(tab_ref[...], hot, preferred_element_type=jnp.float32)
    value = picked[:COLS] + picked[COLS:]
    wanted = lax.broadcasted_iota(jnp.int32, (COLS, TILE), 0) == col
    out_ref[...] = jnp.sum(jnp.where(wanted, value, jnp.float32(0.0)), axis=0, keepdims=True)


def split_table(pheno_full):
    table = pheno_full.reshape(-1, COLS)
    top = lax.reduce_precision(table, exponent_bits=8, mantissa_bits=7)
    rest = table - top
    pieces = [piece.T.astype(jnp.bfloat16) for piece in (top, rest)]
    return jnp.concatenate(pieces, axis=0)


def gather_pheno(pheno_full, index, interpret=False):
    stacked = split_table(pheno_full)
    count = index.size
    flat = index.reshape(1, count)
    out = pl.pallas_call(
        gather_body,
        grid=(count // TILE,),
        in_specs=[
            pl.BlockSpec((1, TILE), lambda i: (0, i)),
            pl.BlockSpec(stacked.shape, lambda i: (0, 0)),
        ],
        out_specs=pl.BlockSpec((1, TILE), lambda i: (0, i)),
        out_shape=jax.ShapeDtypeStruct((1, count), jnp.float32),
        interpret=interpret,
    )(flat, stacked)
    return out.reshape(index.shape)


def doubling_psum(x, axes):
    for axis in axes:
        size = lax.axis_size(axis)
        step = 1
        while step < size:
            pairs = [(i, i ^ step) for i in range(size)]
            x = x + lax.ppermute(x, axis, pairs)
            step *= 2
    return x


def doubling_gather(x, steps):
    for axis, level in steps:
        size = lax.axis_size(axis)
        bit = (lax.axis_index(axis) >> level) & 1
        flip = [(i, i ^ (1 << level)) for i in range(size)]
        other = lax.ppermute(x, axis, flip)
        low = jnp.where(bit == 0, x, other)
        high = jnp.where(bit == 0, other, x)
        x = jnp.concatenate([low, high], axis=0)
    return x


def front_chain(pheno, gram, steps, side, tie_after):
    for index, (axis, level) in enumerate(steps):
        if index == tie_after:
            pheno, gram, side = lax.optimization_barrier((pheno, gram, side))
        size = lax.axis_size(axis)
        bit = (lax.axis_index(axis) >> level) & 1
        flip = [(i, i ^ (1 << level)) for i in range(size)]
        count = pheno.shape[0]
        packed = lax.ppermute(jnp.concatenate([pheno, gram.reshape(-1)]), axis, flip)
        other, other_gram = packed[:count], packed[count:].reshape(gram.shape)
        low = jnp.where(bit == 0, pheno, other)
        high = jnp.where(bit == 0, other, pheno)
        pheno = jnp.concatenate([low, high], axis=0)
        gram = gram + other_gram
    return pheno, gram, side


def axis_bits(axes):
    steps = []
    for axis in axes:
        level = 0
        while (1 << level) < lax.axis_size(axis):
            steps.append((axis, level))
            level += 1
    return steps


def split_bits():
    bits = []
    for axis, count in (("core", 1), ("x", 2), ("z", 3)):
        for level in range(count):
            bits.append((axis, level))
    return bits


def exchange(keep_lo, keep_hi, axis, level, along):
    size = lax.axis_size(axis)
    bit = (lax.axis_index(axis) >> level) & 1
    flip = [(i, i ^ (1 << level)) for i in range(size)]
    send = jnp.where(bit == 0, keep_hi, keep_lo)
    mine = jnp.where(bit == 0, keep_lo, keep_hi)
    return mine + lax.ppermute(send, axis, flip)


def halve_bit(cur, names, name):
    position = len(names) - 1 - names.index(name) + 3
    rows, cols = cur.shape
    axis, level = name
    size = lax.axis_size(axis)
    bit = (lax.axis_index(axis) >> level) & 1
    flip = [(i, i ^ (1 << level)) for i in range(size)]
    split = cur.reshape(rows >> (position + 1), 2, 1 << position, cols)
    low, high = split[:, 0], split[:, 1]
    send = jnp.where(bit == 0, high, low)
    mine = jnp.where(bit == 0, low, high)
    kept = mine + lax.ppermute(send, axis, flip)
    return kept.reshape(rows // 2, cols), [n for n in names if n != name]


def reorder_dosages(genotypes):
    local_rows, variants = genotypes.shape
    nz, nx, nc = (lax.axis_size(a) for a in SAMP)
    own_rows = variants // (nz * nx * nc)
    order = genotypes.reshape(local_rows, 2, 2, 2, 2, 2, nc, own_rows)
    order = order.transpose(0, 6, 5, 4, 3, 2, 1, 7)
    return order.reshape(local_rows, variants).astype(jnp.bfloat16)


def halving_scores(weighted, dosages):
    cur = jnp.dot(weighted.T, dosages, preferred_element_type=jnp.float32)
    half = cur.shape[1] // 2
    cur = exchange(cur[:, :half], cur[:, half:], "core", 0, 1).T
    names = [("x", 0), ("x", 1), ("z", 0), ("z", 1), ("z", 2)]
    cols = cur.shape[1] // 2
    part_a, names_a = cur[:, :cols], list(names)
    part_b, names_b = cur[:, cols:], list(names)
    plan = [(("x", 0), ("z", 0)), (("z", 0), ("x", 0)), (("x", 1), ("z", 1)), (("z", 1), ("x", 1))]
    for step_a, step_b in plan:
        part_a, names_a = halve_bit(part_a, names_a, step_a)
        part_b, names_b = halve_bit(part_b, names_b, step_b)
    cur = jnp.concatenate([part_a, part_b], axis=1)
    cur, _ = halve_bit(cur, names_a, ("z", 2))
    return cur


def per_device(phenotype, exposures, perms, genotypes):
    hi = lax.Precision.HIGHEST
    nv = lax.axis_size("vgrp")
    local_rows = exposures.shape[0]
    width = exposures.shape[1]
    quarter = local_rows // nv
    offset_rows = lax.axis_index("vgrp") * quarter
    expo_part = lax.dynamic_slice_in_dim(exposures, offset_rows, quarter, 0)
    gram_part = jnp.dot(expo_part.T, expo_part, precision=hi)
    steps = axis_bits(("core", "x", "z", "vgrp"))
    pheno_full, gram, dosages = front_chain(phenotype, gram_part, steps, reorder_dosages(genotypes), 5)
    samples = pheno_full.shape[0]
    system = gram + 0.5 * samples * jnp.eye(width, dtype=jnp.float32)
    factor = jnp.linalg.cholesky(system)
    perm_part = lax.dynamic_slice_in_dim(perms, offset_rows, quarter, 1)
    pheno_part = gather_pheno(pheno_full, perm_part).T
    cross_part = jnp.dot(expo_part.T, pheno_part, precision=hi)
    cross = doubling_psum(cross_part, ("core", "x", "z", "vgrp"))
    coefficients = chol_solve(factor, cross)
    permuted = doubling_gather(pheno_part, axis_bits(("vgrp",)))
    residuals = permuted - jnp.dot(exposures, coefficients, precision=hi)
    nperm = residuals.shape[1]
    weighted = (
        (exposures[:, :, None] * residuals[:, None, :])
        .reshape(local_rows, width * nperm)
        .astype(jnp.bfloat16)
    )
    own_scores = halving_scores(weighted, dosages)
    shaped = own_scores.reshape(own_scores.shape[0], width, nperm)
    return jnp.sum(shaped * shaped, axis=1) / (samples * width)


def solution(mesh):
    nv, ns = mesh.devices.shape
    fine = Mesh(mesh.devices.reshape(nv, ns // 8, 4, 2), ALL)
    return jax.shard_map(
        per_device,
        mesh=fine,
        in_specs=(P(ALL), P(SAMP, None), P(None, SAMP), P(SAMP, "vgrp")),
        out_specs=P(ALL, None),
        check_vma=False,
    )
```

```python
import jax
import jax.numpy as jnp
from jax import lax
from jax.experimental import pallas as pl
from jax.sharding import Mesh, PartitionSpec as P

SAMP = ("z", "x", "core")
ALL = ("vgrp",) + SAMP


def chol_solve(factor, rhs):
    middle = lax.linalg.triangular_solve(factor, rhs, left_side=True, lower=True)
    return lax.linalg.triangular_solve(factor, middle, left_side=True, lower=True, transpose_a=True)


COLS = 256
TILE = 1024


def gather_body(idx_ref, tab_ref, out_ref):
    idx = idx_ref[...]
    rows = tab_ref.shape[1]
    row = idx // COLS
    col = idx % COLS
    hot = (lax.broadcasted_iota(jnp.int32, (rows, TILE), 0) == row).astype(jnp.bfloat16)
    picked = jnp.dot(tab_ref[...], hot, preferred_element_type=jnp.float32)
    value = picked[:COLS] + picked[COLS:]
    wanted = lax.broadcasted_iota(jnp.int32, (COLS, TILE), 0) == col
    out_ref[...] = jnp.sum(jnp.where(wanted, value, jnp.float32(0.0)), axis=0, keepdims=True)


def split_table(pheno_full):
    table = pheno_full.reshape(-1, COLS)
    top = lax.reduce_precision(table, exponent_bits=8, mantissa_bits=7)
    rest = table - top
    pieces = [piece.T.astype(jnp.bfloat16) for piece in (top, rest)]
    return jnp.concatenate(pieces, axis=0)


def gather_pheno(pheno_full, index, interpret=False):
    stacked = split_table(pheno_full)
    count = index.size
    flat = index.reshape(1, count)
    out = pl.pallas_call(
        gather_body,
        grid=(count // TILE,),
        in_specs=[
            pl.BlockSpec((1, TILE), lambda i: (0, i)),
            pl.BlockSpec(stacked.shape, lambda i: (0, 0)),
        ],
        out_specs=pl.BlockSpec((1, TILE), lambda i: (0, i)),
        out_shape=jax.ShapeDtypeStruct((1, count), jnp.float32),
        interpret=interpret,
    )(flat, stacked)
    return out.reshape(index.shape)


def doubling_psum(x, axes):
    for axis in axes:
        size = lax.axis_size(axis)
        step = 1
        while step < size:
            pairs = [(i, i ^ step) for i in range(size)]
            x = x + lax.ppermute(x, axis, pairs)
            step *= 2
    return x


def doubling_gather(x, steps):
    for axis, level in steps:
        size = lax.axis_size(axis)
        bit = (lax.axis_index(axis) >> level) & 1
        flip = [(i, i ^ (1 << level)) for i in range(size)]
        other = lax.ppermute(x, axis, flip)
        low = jnp.where(bit == 0, x, other)
        high = jnp.where(bit == 0, other, x)
        x = jnp.concatenate([low, high], axis=0)
    return x


def front_chain(pheno, gram, steps, side, tie_after):
    for index, (axis, level) in enumerate(steps):
        if index == tie_after:
            pheno, gram, side = lax.optimization_barrier((pheno, gram, side))
        size = lax.axis_size(axis)
        bit = (lax.axis_index(axis) >> level) & 1
        flip = [(i, i ^ (1 << level)) for i in range(size)]
        count = pheno.shape[0]
        packed = lax.ppermute(jnp.concatenate([pheno, gram.reshape(-1)]), axis, flip)
        other, other_gram = packed[:count], packed[count:].reshape(gram.shape)
        low = jnp.where(bit == 0, pheno, other)
        high = jnp.where(bit == 0, other, pheno)
        pheno = jnp.concatenate([low, high], axis=0)
        gram = gram + other_gram
    return pheno, gram, side


def axis_bits(axes):
    steps = []
    for axis in axes:
        level = 0
        while (1 << level) < lax.axis_size(axis):
            steps.append((axis, level))
            level += 1
    return steps


def split_bits():
    bits = []
    for axis, count in (("core", 1), ("x", 2), ("z", 3)):
        for level in range(count):
            bits.append((axis, level))
    return bits


def exchange(keep_lo, keep_hi, axis, level, along):
    size = lax.axis_size(axis)
    bit = (lax.axis_index(axis) >> level) & 1
    flip = [(i, i ^ (1 << level)) for i in range(size)]
    send = jnp.where(bit == 0, keep_hi, keep_lo)
    mine = jnp.where(bit == 0, keep_lo, keep_hi)
    return mine + lax.ppermute(send, axis, flip)


def halve_bit(cur, names, name):
    position = len(names) - 1 - names.index(name) + 3
    rows, cols = cur.shape
    axis, level = name
    size = lax.axis_size(axis)
    bit = (lax.axis_index(axis) >> level) & 1
    flip = [(i, i ^ (1 << level)) for i in range(size)]
    split = cur.reshape(rows >> (position + 1), 2, 1 << position, cols)
    low, high = split[:, 0], split[:, 1]
    send = jnp.where(bit == 0, high, low)
    mine = jnp.where(bit == 0, low, high)
    kept = mine + lax.ppermute(send, axis, flip)
    return kept.reshape(rows // 2, cols), [n for n in names if n != name]


def reorder_dosages(genotypes):
    local_rows, variants = genotypes.shape
    nz, nx, nc = (lax.axis_size(a) for a in SAMP)
    own_rows = variants // (nz * nx * nc)
    order = genotypes.reshape(local_rows, 2, 2, 2, 2, 2, nc, own_rows)
    order = order.transpose(0, 6, 5, 4, 3, 2, 1, 7)
    return order.reshape(local_rows, variants).astype(jnp.bfloat16)


def halving_scores(weighted, dosages):
    cur = jnp.dot(weighted.T, dosages, preferred_element_type=jnp.float32)
    half = cur.shape[1] // 2
    cur = exchange(cur[:, :half], cur[:, half:], "core", 0, 1).T
    names = [("x", 0), ("x", 1), ("z", 0), ("z", 1), ("z", 2)]
    cols = cur.shape[1] // 2
    part_a, names_a = cur[:, :cols], list(names)
    part_b, names_b = cur[:, cols:], list(names)
    plan = [(("x", 0), ("z", 0)), (("z", 0), ("x", 0)), (("x", 1), ("z", 1)), (("z", 1), ("x", 1))]
    for step_a, step_b in plan:
        part_a, names_a = halve_bit(part_a, names_a, step_a)
        part_b, names_b = halve_bit(part_b, names_b, step_b)
    cur = jnp.concatenate([part_a, part_b], axis=1)
    cur, _ = halve_bit(cur, names_a, ("z", 2))
    return cur


def per_device(phenotype, exposures, perms, genotypes):
    hi = lax.Precision.HIGHEST
    nv = lax.axis_size("vgrp")
    local_rows = exposures.shape[0]
    width = exposures.shape[1]
    quarter = local_rows // nv
    offset_rows = lax.axis_index("vgrp") * quarter
    expo_part = lax.dynamic_slice_in_dim(exposures, offset_rows, quarter, 0)
    gram_part = jnp.dot(expo_part.T, expo_part, precision=hi)
    steps = axis_bits(("core", "x", "z", "vgrp"))
    pheno_full, gram, dosages = front_chain(phenotype, gram_part, steps, reorder_dosages(genotypes), 7)
    samples = pheno_full.shape[0]
    system = gram + 0.5 * samples * jnp.eye(width, dtype=jnp.float32)
    factor = jnp.linalg.cholesky(system)
    perm_part = lax.dynamic_slice_in_dim(perms, offset_rows, quarter, 1)
    pheno_part = gather_pheno(pheno_full, perm_part).T
    cross_part = jnp.dot(expo_part.T, pheno_part, precision=hi)
    cross = doubling_psum(cross_part, ("core", "x", "z", "vgrp"))
    coefficients = chol_solve(factor, cross)
    permuted = doubling_gather(pheno_part, axis_bits(("vgrp",)))
    residuals = permuted - jnp.dot(exposures, coefficients, precision=hi)
    nperm = residuals.shape[1]
    weighted = (
        (exposures[:, :, None] * residuals[:, None, :])
        .reshape(local_rows, width * nperm)
        .astype(jnp.bfloat16)
    )
    own_scores = halving_scores(weighted, dosages)
    shaped = own_scores.reshape(own_scores.shape[0], width, nperm)
    return jnp.sum(shaped * shaped, axis=1) / (samples * width)


def solution(mesh):
    nv, ns = mesh.devices.shape
    fine = Mesh(mesh.devices.reshape(nv, ns // 8, 4, 2), ALL)
    return jax.shard_map(
        per_device,
        mesh=fine,
        in_specs=(P(ALL), P(SAMP, None), P(None, SAMP), P(SAMP, "vgrp")),
        out_specs=P(ALL, None),
        check_vma=False,
    )
```

```python
import jax
import jax.numpy as jnp
from jax import lax
from jax.experimental import pallas as pl
from jax.sharding import Mesh, PartitionSpec as P

SAMP = ("z", "x", "core")
ALL = ("vgrp",) + SAMP


def chol_solve(factor, rhs):
    middle = lax.linalg.triangular_solve(factor, rhs, left_side=True, lower=True)
    return lax.linalg.triangular_solve(factor, middle, left_side=True, lower=True, transpose_a=True)


COLS = 256
TILE = 1024


def gather_body(idx_ref, tab_ref, out_ref):
    idx = idx_ref[...]
    rows = tab_ref.shape[1]
    row = idx // COLS
    col = idx % COLS
    hot = (lax.broadcasted_iota(jnp.int32, (rows, TILE), 0) == row).astype(jnp.bfloat16)
    picked = jnp.dot(tab_ref[...], hot, preferred_element_type=jnp.float32)
    value = picked[:COLS] + picked[COLS:]
    wanted = lax.broadcasted_iota(jnp.int32, (COLS, TILE), 0) == col
    out_ref[...] = jnp.sum(jnp.where(wanted, value, jnp.float32(0.0)), axis=0, keepdims=True)


def split_table(pheno_full):
    table = pheno_full.reshape(-1, COLS)
    top = lax.reduce_precision(table, exponent_bits=8, mantissa_bits=7)
    rest = table - top
    pieces = [piece.T.astype(jnp.bfloat16) for piece in (top, rest)]
    return jnp.concatenate(pieces, axis=0)


def gather_pheno(pheno_full, index, interpret=False):
    stacked = split_table(pheno_full)
    count = index.size
    flat = index.reshape(1, count)
    out = pl.pallas_call(
        gather_body,
        grid=(count // TILE,),
        in_specs=[
            pl.BlockSpec((1, TILE), lambda i: (0, i)),
            pl.BlockSpec(stacked.shape, lambda i: (0, 0)),
        ],
        out_specs=pl.BlockSpec((1, TILE), lambda i: (0, i)),
        out_shape=jax.ShapeDtypeStruct((1, count), jnp.float32),
        interpret=interpret,
    )(flat, stacked)
    return out.reshape(index.shape)


def doubling_psum(x, axes):
    for axis in axes:
        size = lax.axis_size(axis)
        step = 1
        while step < size:
            pairs = [(i, i ^ step) for i in range(size)]
            x = x + lax.ppermute(x, axis, pairs)
            step *= 2
    return x


def doubling_gather(x, steps):
    for axis, level in steps:
        size = lax.axis_size(axis)
        bit = (lax.axis_index(axis) >> level) & 1
        flip = [(i, i ^ (1 << level)) for i in range(size)]
        other = lax.ppermute(x, axis, flip)
        low = jnp.where(bit == 0, x, other)
        high = jnp.where(bit == 0, other, x)
        x = jnp.concatenate([low, high], axis=0)
    return x


def front_chain(pheno, gram, steps, side, tie_after):
    for index, (axis, level) in enumerate(steps):
        if index == tie_after:
            pheno, gram, side = lax.optimization_barrier((pheno, gram, side))
        size = lax.axis_size(axis)
        bit = (lax.axis_index(axis) >> level) & 1
        flip = [(i, i ^ (1 << level)) for i in range(size)]
        count = pheno.shape[0]
        packed = lax.ppermute(jnp.concatenate([pheno, gram.reshape(-1)]), axis, flip)
        other, other_gram = packed[:count], packed[count:].reshape(gram.shape)
        low = jnp.where(bit == 0, pheno, other)
        high = jnp.where(bit == 0, other, pheno)
        pheno = jnp.concatenate([low, high], axis=0)
        gram = gram + other_gram
    return pheno, gram, side


def axis_bits(axes):
    steps = []
    for axis in axes:
        level = 0
        while (1 << level) < lax.axis_size(axis):
            steps.append((axis, level))
            level += 1
    return steps


def split_bits():
    bits = []
    for axis, count in (("core", 1), ("x", 2), ("z", 3)):
        for level in range(count):
            bits.append((axis, level))
    return bits


def exchange(keep_lo, keep_hi, axis, level, along):
    size = lax.axis_size(axis)
    bit = (lax.axis_index(axis) >> level) & 1
    flip = [(i, i ^ (1 << level)) for i in range(size)]
    send = jnp.where(bit == 0, keep_hi, keep_lo)
    mine = jnp.where(bit == 0, keep_lo, keep_hi)
    return mine + lax.ppermute(send, axis, flip)


def halve_bit(cur, names, name):
    position = len(names) - 1 - names.index(name) + 3
    rows, cols = cur.shape
    axis, level = name
    size = lax.axis_size(axis)
    bit = (lax.axis_index(axis) >> level) & 1
    flip = [(i, i ^ (1 << level)) for i in range(size)]
    split = cur.reshape(rows >> (position + 1), 2, 1 << position, cols)
    low, high = split[:, 0], split[:, 1]
    send = jnp.where(bit == 0, high, low)
    mine = jnp.where(bit == 0, low, high)
    kept = mine + lax.ppermute(send, axis, flip)
    return kept.reshape(rows // 2, cols), [n for n in names if n != name]


def reorder_dosages(genotypes):
    local_rows, variants = genotypes.shape
    nz, nx, nc = (lax.axis_size(a) for a in SAMP)
    own_rows = variants // (nz * nx * nc)
    order = genotypes.reshape(local_rows, 2, 2, 2, 2, 2, nc, own_rows)
    order = order.transpose(0, 6, 5, 4, 3, 2, 1, 7)
    return order.reshape(local_rows, variants).astype(jnp.bfloat16)


def halving_scores(weighted, dosages):
    cur = jnp.dot(weighted.T, dosages, preferred_element_type=jnp.float32)
    half = cur.shape[1] // 2
    cur = exchange(cur[:, :half], cur[:, half:], "core", 0, 1).T
    names = [("x", 0), ("x", 1), ("z", 0), ("z", 1), ("z", 2)]
    cols = cur.shape[1] // 2
    part_a, names_a = cur[:, :cols], list(names)
    part_b, names_b = cur[:, cols:], list(names)
    plan = [(("x", 0), ("z", 0)), (("z", 0), ("x", 0)), (("x", 1), ("z", 1)), (("z", 1), ("x", 1))]
    for step_a, step_b in plan:
        part_a, names_a = halve_bit(part_a, names_a, step_a)
        part_b, names_b = halve_bit(part_b, names_b, step_b)
    cur = jnp.concatenate([part_a, part_b], axis=1)
    cur, _ = halve_bit(cur, names_a, ("z", 2))
    return cur


def per_device(phenotype, exposures, perms, genotypes):
    hi = lax.Precision.HIGHEST
    nv = lax.axis_size("vgrp")
    local_rows = exposures.shape[0]
    width = exposures.shape[1]
    quarter = local_rows // nv
    offset_rows = lax.axis_index("vgrp") * quarter
    expo_part = lax.dynamic_slice_in_dim(exposures, offset_rows, quarter, 0)
    gram_part = jnp.dot(expo_part.T, expo_part, precision=hi)
    steps = axis_bits(("core", "x", "z", "vgrp"))
    pheno_full, gram, dosages = front_chain(phenotype, gram_part, steps, reorder_dosages(genotypes), 5)
    samples = pheno_full.shape[0]
    system = gram + 0.5 * samples * jnp.eye(width, dtype=jnp.float32)
    factor = jnp.linalg.cholesky(system)
    inverse = chol_solve(factor, jnp.eye(width, dtype=jnp.float32))
    perm_part = lax.dynamic_slice_in_dim(perms, offset_rows, quarter, 1)
    pheno_part = gather_pheno(pheno_full, perm_part).T
    cross_part = jnp.dot(expo_part.T, pheno_part, precision=hi)
    cross = doubling_psum(cross_part, ("core", "x", "z", "vgrp"))
    coefficients = jnp.dot(inverse, cross, precision=hi)
    permuted = doubling_gather(pheno_part, axis_bits(("vgrp",)))
    residuals = permuted - jnp.dot(exposures, coefficients, precision=hi)
    nperm = residuals.shape[1]
    weighted = (
        (exposures[:, :, None] * residuals[:, None, :])
        .reshape(local_rows, width * nperm)
        .astype(jnp.bfloat16)
    )
    own_scores = halving_scores(weighted, dosages)
    shaped = own_scores.reshape(own_scores.shape[0], width, nperm)
    return jnp.sum(shaped * shaped, axis=1) / (samples * width)


def solution(mesh):
    nv, ns = mesh.devices.shape
    fine = Mesh(mesh.devices.reshape(nv, ns // 8, 4, 2), ALL)
    return jax.shard_map(
        per_device,
        mesh=fine,
        in_specs=(P(ALL), P(SAMP, None), P(None, SAMP), P(SAMP, "vgrp")),
        out_specs=P(ALL, None),
        check_vma=False,
    )
```
